256 devices in a mesh: dp: 16 (over y, x), expert: 16 (over z, core).
Axes of the slice: x: 4, y: 4, z: 8, core: 2. Of those that a mesh axis runs over, the one named last changes fastest.
Arguments:
- tokens: bfloat16 [49152, 3584], P(('dp', 'expert')), may hold values from -24 to 24
- cotangent: bfloat16 [49152, 3584], P(('dp', 'expert')), may hold values from -0.078125 to 0.078125
- probs: float32 [49152, 2], P(('dp', 'expert')), may hold values from 0.1 to 1
- expert_ids: int32 [49152, 2], P(('dp', 'expert')), may hold values from 0 to 15, all different within a row; in each aligned block of 192 rows (0 to 191, 192 to 383, ...) at most 25 rows name the same one
- w_up: bfloat16 [16, 3584, 1024], P('expert', 'dp'), may hold values from -0.09375 to 0.09375
- w_down: bfloat16 [16, 1024, 3584], P('expert', 'dp'), may hold values from -0.1875 to 0.1875
Outputs:
- grad_up: float32 [16, 3584, 1024], P('expert', 'dp')
- grad_down: float32 [16, 1024, 3584], P('expert', 'dp')
The draws below stay inside these ranges and needn't reach their ends.
Inputs may be any that keep to these rules, and one draw needn't show every extreme that they name: `expert_ids`: each row names 2 different experts. Among the rows of one device no expert is named by more than 25 rows, and in every draw some device has an expert named by exactly 25 rows.
All inputs are finite; a program needn't handle non-finite values.
Results may differ from the reference program's by a relative error of at most 0.017.
Values may be sent and summed in bfloat16 or wider, within the bound.
No kernel may reach another device: no remote copies, remote signals or barrier semaphores. Data moves between devices by JAX's collectives and lax.ppermute only.
A program may use at most 128 MiB of HBM per device.

```python
import math
import jax
import jax.numpy as jnp
import numpy as np
from jax import lax

D = 3584
FF = 1024
TOPK = 2
TOK_DEV = 192
EXPERTS = 16
CAP = 25
TOKENS = 49152
N_DP = 16
N_EXPERT = 16


def strengthened(entries, rng, source, target, shards_of, factor):
    def block_of(axis_at):
        return (jnp.arange(entries.shape[axis_at]) // (entries.shape[axis_at] // shards_of)).reshape((-1,) + (1,) * (entries.ndim - 1 - axis_at))

    one_side = jax.random.permutation(rng, shards_of)[block_of(target)]
    far = (block_of(target) + shards_of // 2) % shards_of
    return jnp.where((block_of(source) == one_side) | (block_of(source) == far), factor * entries, entries)


def level_of(stream_key, shape, split, smallest, top_value):
    loudness, own = 1.0, jax.random.fold_in(stream_key, 6)
    for axis_at, shards_of in split:
        draws = jnp.exp(jax.random.uniform(jax.random.fold_in(own, axis_at), (shards_of,), jnp.float32, smallest / len(split), top_value / len(split)))
        loudness = loudness * jnp.repeat(draws, shape[axis_at] // shards_of).reshape([-1 if axis == axis_at else 1 for axis in range(len(shape))])
    return loudness


def routed_block(stream_key, own, number, rows, number_of, top, most, skew):
    order = jax.random.permutation(stream_key, number_of)
    packed, ordinary = load_shares(number_of, rows * top, most, skew, True), load_shares(number_of, rows * top, most, skew, False)
    places = jnp.arange(number_of)

    def named(sizes, offset_by):
        used = int((sizes > 0).sum())
        fixed = max(1, used // 4)
        moved = fixed + (places - fixed + offset_by * (used - fixed)) % max(1, number_of - fixed)
        return jnp.zeros((number_of,), jnp.int32).at[order[jnp.where(places < fixed, places, moved)]].set(jnp.asarray(sizes, jnp.int32))

    sizes = jnp.where(number % 4 == 0, named(packed, number // 4), named(ordinary, number - number // 4 - 1))
    mixed = jax.random.permutation(jax.random.fold_in(own, 3), number_of)
    source_of, sink = mixed[0:number_of // 2 * 2:2], mixed[1:number_of // 2 * 2:2]
    slack = jnp.minimum(sizes[source_of] - 1, most - sizes[sink]) // 2
    slack = jnp.where((source_of == order[0]) | (sink == order[0]) | (sizes[sink] == 0), 0, jnp.maximum(slack, 0))
    moved = jax.random.randint(jax.random.fold_in(own, 4), (number_of // 2,), 0, 1 << 20) % (slack + 1)
    sizes = sizes.at[source_of].add(-moved).at[sink].add(moved)
    labels = jnp.searchsorted(jnp.cumsum(sizes), jnp.arange(rows * top), side="right").astype(jnp.int32)
    table = labels.reshape(top, rows).T
    table = table[jax.random.permutation(jax.random.fold_in(own, 1), rows)]
    offset_by = jax.random.randint(jax.random.fold_in(own, 2), (rows, 1), 0, top)
    return jnp.take_along_axis(table, (jnp.arange(top)[None, :] + offset_by) % top, axis=1)


def load_shares(count, total, most, slope, full):
    portions = [(1 << 20) // math.isqrt(rank ** slope) + 1 for rank in range(1, count + 1)]
    largest = most if full else min(most, max(-(-total // count), total * portions[0] // sum(portions)))
    least = 1 if total - largest >= count - 1 else 0
    given, surplus = [largest] + [least] * (count - 1), total - largest - least * (count - 1)
    while surplus > 0:
        candidates = [i for i in range(1, count) if given[i] < largest] or [i for i in range(1, count) if given[i] < most]
        whole, budget = sum([portions[i] for i in candidates]), surplus
        for i in candidates:
            extra = min(most - given[i], max(1, budget * portions[i] // whole), surplus)
            given[i] = given[i] + extra
            surplus = surplus - extra
    return np.array(given)


def centred(key, shape, width, limit, shards=(), kind=jnp.bfloat16):
    factor_of = level_of(key, shape, shards, -0.22, 0.18) if shards else 1.0
    result = jax.random.normal(key, shape, jnp.float32) * width * factor_of
    return jnp.minimum(jnp.maximum(result, -limit), limit).astype(kind)


def heavy_noise(key, shape, deviation, reach, cuts, heavy, held_as=jnp.bfloat16):
    drawn = deviation * jax.random.normal(key, shape, jnp.float32)
    if cuts:
        drawn = drawn * level_of(key, shape, cuts, -0.22, 0.18)
    return jnp.clip(strengthened(drawn, jax.random.fold_in(key, 3), *heavy), -reach, reach).astype(held_as)


def setup_inputs(seed: int = 0) -> dict:
    streams_of = jax.random.split(jax.random.key(seed), 7)
    tokens = heavy_noise(streams_of[0], (TOKENS, D), 1.0, 24.0, ((0, 256),), (0, 1, 256, 6.0))
    cotangent = centred(streams_of[1], (TOKENS, D), ((2.0 * TOK_DEV * N_DP) ** -0.5), 0.078125, ((0, 256),))
    probs = jnp.clip(0.1 + 0.9 * jax.random.uniform(streams_of[2], (TOKENS, TOPK), jnp.float32) ** level_of(streams_of[2], (TOKENS, TOPK), ((0, 256),), -0.2, 0.2), 0.1, 1.0)
    expert_ids_keys = jax.random.split(jax.random.fold_in(streams_of[3], 1), TOKENS // TOK_DEV)
    expert_ids_turns = jax.random.permutation(jax.random.fold_in(streams_of[3], 3), TOKENS // TOK_DEV)
    expert_ids = jax.vmap(lambda own, number: routed_block(jax.random.fold_in(streams_of[3], 2), own, number, TOK_DEV, EXPERTS, TOPK, CAP, 2))(expert_ids_keys, expert_ids_turns).reshape((TOKENS, TOPK))
    w_up = centred(streams_of[4], (EXPERTS, D, FF), D ** -0.5, 0.09375, ((0, 16), (1, 16)))
    w_down = centred(streams_of[5], (EXPERTS, FF, D), FF ** -0.5, 0.1875, ((0, 16), (1, 16)))
    return {"tokens": tokens, "cotangent": cotangent, "probs": probs, "expert_ids": expert_ids, "w_up": w_up, "w_down": w_down}


def slot_index(choice_ids):
    flat = choice_ids.reshape(-1)
    onehot = (flat[:, None] == jnp.arange(EXPERTS, dtype=jnp.int32)[None, :]).astype(jnp.int32)
    before = jnp.cumsum(onehot, axis=0) - onehot
    ranked = jnp.sum(before * onehot, axis=1).astype(jnp.int32)
    return (flat * CAP + ranked).reshape(-1, TOPK)


def expert_rows(tok_block, cot_block, prob_block, id_block, expert_num):
    slot_of = slot_index(id_block)
    wanted = expert_num * CAP + jnp.arange(CAP, dtype=jnp.int32)
    matches = wanted[:, None, None] == slot_of[None, :, :]
    placing = jnp.any(matches, axis=2).astype(jnp.bfloat16)
    factor = jnp.sum(jnp.where(matches, prob_block[None, :, :], jnp.float32(0.0)), axis=(1, 2))
    x_rows = jnp.dot(placing, tok_block, preferred_element_type=jnp.float32).astype(jnp.bfloat16)
    cot_rows = jnp.dot(placing, cot_block, preferred_element_type=jnp.float32)
    g_rows = (cot_rows * factor[:, None]).astype(jnp.bfloat16)
    return x_rows, g_rows


def partials(x_rows, g_rows, up_mat, down_mat):
    pre = jnp.dot(x_rows, up_mat, preferred_element_type=jnp.float32)
    sigmoid_pre = jax.nn.sigmoid(pre)
    hidden = (pre * sigmoid_pre).astype(jnp.bfloat16)
    part_down = jnp.dot(hidden.T, g_rows, preferred_element_type=jnp.float32)
    hidden_grad = jnp.dot(g_rows, down_mat.T, preferred_element_type=jnp.float32)
    pre_grad = (hidden_grad * (sigmoid_pre * (1.0 + pre * (1.0 - sigmoid_pre)))).astype(jnp.bfloat16)
    part_up = jnp.dot(x_rows.T, pre_grad, preferred_element_type=jnp.float32)
    rounded_up = lax.optimization_barrier(part_up.astype(jnp.bfloat16)).astype(jnp.float32)
    rounded_down = lax.optimization_barrier(part_down.astype(jnp.bfloat16)).astype(jnp.float32)
    return rounded_up, rounded_down


def reference(tokens, cotangent, probs, expert_ids, w_up, w_down):
    tok_all = tokens.reshape(N_DP, N_EXPERT, TOK_DEV, D)
    cot_all = cotangent.reshape(N_DP, N_EXPERT, TOK_DEV, D)
    prob_all = probs.reshape(N_DP, N_EXPERT, TOK_DEV, TOPK)
    ids_all = expert_ids.reshape(N_DP, N_EXPERT, TOK_DEV, TOPK)

    def per_expert(expert_num):
        up_mat = w_up[expert_num]
        down_mat = w_down[expert_num]

        def per_group(carry, group):
            def one_block(tok_block, cot_block, prob_block, id_block):
                return expert_rows(tok_block, cot_block, prob_block, id_block, expert_num)

            x_rows, g_rows = jax.vmap(one_block)(tok_all[group], cot_all[group], prob_all[group], ids_all[group])
            part_up, part_down = partials(x_rows.reshape(-1, D), g_rows.reshape(-1, D), up_mat, down_mat)
            return (carry[0] + part_up, carry[1] + part_down), None

        start = (jnp.zeros((D, FF), jnp.float32), jnp.zeros((FF, D), jnp.float32))
        totals, unused = lax.scan(per_group, start, jnp.arange(N_DP, dtype=jnp.int32))
        return totals

    grad_up, grad_down = lax.map(per_expert, jnp.arange(EXPERTS, dtype=jnp.int32))
    return grad_up, grad_down
```

```python
import math

import jax
import jax.numpy as jnp
from jax import lax
from jax.sharding import PartitionSpec as P


def slot_positions(choice_ids, capacity, experts):
    flat = choice_ids.reshape(-1)
    onehot = (flat[:, None] == jnp.arange(experts, dtype=jnp.int32)[None, :]).astype(jnp.int32)
    before = jnp.cumsum(onehot, axis=0) - onehot
    ranked = jnp.sum(before * onehot, axis=1)
    return (flat * capacity + ranked).reshape(choice_ids.shape)


def ring_perms(n_x, n_y):
    def idx(y, x):
        return y * n_x + x

    x_fwd = [(idx(y, x), idx(y, (x + 1) % n_x)) for y in range(n_y) for x in range(n_x)]
    x_bwd = [(idx(y, x), idx(y, (x - 1) % n_x)) for y in range(n_y) for x in range(n_x)]
    y_fwd = [(idx(y, x), idx((y + 1) % n_y, x)) for y in range(n_y) for x in range(n_x)]
    y_bwd = [(idx(y, x), idx((y - 1) % n_y, x)) for y in range(n_y) for x in range(n_x)]
    return {"x": (x_fwd, x_bwd), "y": (y_fwd, y_bwd)}


class RingRS:
    def __init__(self, chunks, axis, pos, n, perms):
        self.chunks, self.axis, self.pos, self.n = chunks, axis, pos, n
        self.fwd, self.bwd = perms
        half = chunks.shape[-1] // 2
        self.half = half
        self.s = 0
        self.acc_f = self.take((pos - 1) % n, 0)
        self.acc_b = self.take((pos + 1) % n, 1)

    def take(self, i, side):
        blk = lax.dynamic_index_in_dim(self.chunks, i, self.axis, keepdims=False)
        return blk[..., side * self.half:(side + 1) * self.half]

    def step(self):
        s, pos, n = self.s, self.pos, self.n
        got_f = lax.ppermute(self.acc_f.astype(jnp.bfloat16), "dp", self.fwd)
        got_b = lax.ppermute(self.acc_b.astype(jnp.bfloat16), "dp", self.bwd)
        self.acc_f = self.take((pos - s - 2) % n, 0) + got_f.astype(jnp.float32)
        self.acc_b = self.take((pos + s + 2) % n, 1) + got_b.astype(jnp.float32)
        self.s += 1

    def result(self):
        return jnp.concatenate([self.acc_f, self.acc_b], axis=-1)


def reduce_scatter_2d(part_a, part_b, n_x, n_y):
    dp = lax.axis_index("dp")
    px, py = dp % n_x, dp // n_x
    perms = ring_perms(n_x, n_y)
    a = part_a.reshape(n_y, n_x, part_a.shape[0] // (n_x * n_y), part_a.shape[1])
    b = part_b.reshape(n_y, n_x, part_b.shape[0] // (n_x * n_y), part_b.shape[1])
    ra = RingRS(a, 1, px, n_x, perms["x"])
    rb = RingRS(b, 0, py, n_y, perms["y"])
    for _ in range(max(n_x, n_y) - 1):
        if ra.s < n_x - 1:
            ra.step()
        if rb.s < n_y - 1:
            rb.step()
    a1 = ra.result()
    b1 = rb.result()
    ra2 = RingRS(a1, 0, py, n_y, perms["y"])
    rb2 = RingRS(b1, 0, px, n_x, perms["x"])
    for _ in range(max(n_x, n_y) - 1):
        if ra2.s < n_y - 1:
            ra2.step()
        if rb2.s < n_x - 1:
            rb2.step()
    return ra2.result(), rb2.result()


def body(tokens, cotangent, probs, expert_ids, w_up, w_down, n_x, n_y):
    tok_count, model_width = tokens.shape
    experts = lax.axis_size("expert")
    capacity = 2 * tok_count // experts + 1
    slot_of = slot_positions(expert_ids, capacity, experts)
    slot_ids = jnp.arange(experts * capacity, dtype=jnp.int32)
    matches = slot_ids[:, None, None] == slot_of[None, :, :]
    placing = jnp.any(matches, axis=2).astype(jnp.bfloat16)
    factor = jnp.sum(jnp.where(matches, probs[None, :, :], jnp.float32(0.0)), axis=(1, 2))
    x_slots = jnp.dot(placing, tokens, preferred_element_type=jnp.float32).astype(jnp.bfloat16)
    cot_slots = jnp.dot(placing, cotangent, preferred_element_type=jnp.float32)
    scaled = (cot_slots * factor[:, None]).astype(jnp.bfloat16)
    slot_shape = (experts, capacity, model_width)
    got_inputs, got_grads = (
        lax.all_to_all(
            x_slots.reshape(slot_shape), "expert", split_axis=0, concat_axis=0, tiled=True
        ),
        lax.all_to_all(
            scaled.reshape(slot_shape), "expert", split_axis=0, concat_axis=0, tiled=True
        ),
    )
    inputs = got_inputs.reshape(-1, model_width)
    grads_in = got_grads.reshape(-1, model_width)
    up_local = w_up[0]
    down_local = w_down[0]
    up_full, down_full = (
        lax.all_gather(up_local, "dp", axis=0, tiled=True),
        lax.all_gather(down_local, "dp", axis=0, tiled=True),
    )
    pre = jnp.dot(inputs, up_full, preferred_element_type=jnp.float32)
    sigmoid_pre = jax.nn.sigmoid(pre)
    hidden = (pre * sigmoid_pre).astype(jnp.bfloat16)
    hidden_grad = lax.dot_general(
        grads_in, down_full, (((1,), (1,)), ((), ())), preferred_element_type=jnp.float32
    )
    pre_grad = (hidden_grad * (sigmoid_pre * (1.0 + pre * (1.0 - sigmoid_pre)))).astype(
        jnp.bfloat16
    )
    part_up = lax.dot_general(
        inputs, pre_grad, (((0,), (0,)), ((), ())), preferred_element_type=jnp.float32
    ).astype(jnp.bfloat16).astype(jnp.float32)
    part_down = lax.dot_general(
        hidden, grads_in, (((0,), (0,)), ((), ())), preferred_element_type=jnp.float32
    ).astype(jnp.bfloat16).astype(jnp.float32)
    grad_up, grad_down = reduce_scatter_2d(part_up, part_down, n_x, n_y)
    return (grad_up[None], grad_down[None])


def solution(mesh):
    n_dp = mesh.shape["dp"]
    n_x = math.isqrt(n_dp)
    n_y = n_dp // n_x
    in_specs = (
        P(("dp", "expert"), None),
        P(("dp", "expert"), None),
        P(("dp", "expert"), None),
        P(("dp", "expert"), None),
        P("expert", "dp", None),
        P("expert", "dp", None),
    )
    out_specs = (P("expert", "dp", None), P("expert", "dp", None))

    def fn(*args):
        return body(*args, n_x=n_x, n_y=n_y)

    return jax.shard_map(fn, mesh=mesh, in_specs=in_specs, out_specs=out_specs, check_vma=False)
```

```python
import math

import jax
import jax.numpy as jnp
from jax import lax
from jax.sharding import PartitionSpec as P


def slot_positions(choice_ids, capacity, experts):
    flat = choice_ids.reshape(-1)
    onehot = (flat[:, None] == jnp.arange(experts, dtype=jnp.int32)[None, :]).astype(jnp.int32)
    before = jnp.cumsum(onehot, axis=0) - onehot
    ranked = jnp.sum(before * onehot, axis=1)
    return (flat * capacity + ranked).reshape(choice_ids.shape)


def ring_perms(n_x, n_y):
    def idx(y, x):
        return y * n_x + x

    x_fwd = [(idx(y, x), idx(y, (x + 1) % n_x)) for y in range(n_y) for x in range(n_x)]
    x_bwd = [(idx(y, x), idx(y, (x - 1) % n_x)) for y in range(n_y) for x in range(n_x)]
    y_fwd = [(idx(y, x), idx((y + 1) % n_y, x)) for y in range(n_y) for x in range(n_x)]
    y_bwd = [(idx(y, x), idx((y - 1) % n_y, x)) for y in range(n_y) for x in range(n_x)]
    return {"x": (x_fwd, x_bwd), "y": (y_fwd, y_bwd)}


class RingRS:
    def __init__(self, chunks, pos, n, perms):
        h = chunks.shape[1] // 2
        self.lo, self.hi = chunks[:, :h], chunks[:, h:]
        self.pos, self.n = pos, n
        self.fwd, self.bwd = perms
        self.s = 0
        self.acc_f = self.take(self.lo, (pos - 1) % n)
        self.acc_b = self.take(self.hi, (pos + 1) % n)

    @staticmethod
    def take(part, i):
        return lax.dynamic_index_in_dim(part, i, 0, keepdims=False).astype(jnp.float32)

    def step(self):
        s, pos, n = self.s, self.pos, self.n
        got_f = lax.ppermute(self.acc_f.astype(jnp.bfloat16), "dp", self.fwd)
        got_b = lax.ppermute(self.acc_b.astype(jnp.bfloat16), "dp", self.bwd)
        self.acc_f = self.take(self.lo, (pos - s - 2) % n) + got_f.astype(jnp.float32)
        self.acc_b = self.take(self.hi, (pos + s + 2) % n) + got_b.astype(jnp.float32)
        self.s += 1

    def result(self):
        return jnp.concatenate([self.acc_f, self.acc_b], axis=0)


def run_rings(ring_a, ring_b):
    while ring_a.s < ring_a.n - 1 or ring_b.s < ring_b.n - 1:
        if ring_a.s < ring_a.n - 1:
            ring_a.step()
        if ring_b.s < ring_b.n - 1:
            ring_b.step()
    return ring_a.result(), ring_b.result()


def reduce_scatter_2d(part_up, part_down_xy, n_x, n_y):
    dp = lax.axis_index("dp")
    px, py = dp % n_x, dp // n_x
    perms = ring_perms(n_x, n_y)
    up1, down1 = run_rings(
        RingRS(part_up, py, n_y, perms["y"]), RingRS(part_down_xy, px, n_x, perms["x"])
    )
    return run_rings(RingRS(up1, px, n_x, perms["x"]), RingRS(down1, py, n_y, perms["y"]))


def body(tokens, cotangent, probs, expert_ids, w_up, w_down, n_x, n_y):
    tok_count, model_width = tokens.shape
    experts = lax.axis_size("expert")
    capacity = 2 * tok_count // experts + 1
    slot_of = slot_positions(expert_ids, capacity, experts)
    slot_ids = jnp.arange(experts * capacity, dtype=jnp.int32)
    matches = slot_ids[:, None, None] == slot_of[None, :, :]
    placing = jnp.any(matches, axis=2).astype(jnp.bfloat16)
    factor = jnp.sum(jnp.where(matches, probs[None, :, :], jnp.float32(0.0)), axis=(1, 2))
    x_slots = jnp.dot(placing, tokens, preferred_element_type=jnp.float32).astype(jnp.bfloat16)
    cot_slots = jnp.dot(placing, cotangent, preferred_element_type=jnp.float32)
    scaled = (cot_slots * factor[:, None]).astype(jnp.bfloat16)
    both = jnp.concatenate(
        [x_slots.reshape(experts, capacity, model_width), scaled.reshape(experts, capacity, model_width)],
        axis=1,
    )
    per_expert = 2 * capacity * model_width
    lanes = 128 if per_expert % (128 * 8) == 0 else model_width
    got = lax.all_to_all(
        both.reshape(experts, per_expert // lanes, lanes), "expert", split_axis=0, concat_axis=0, tiled=True
    ).reshape(experts, 2 * capacity, model_width)
    inputs = got[:, :capacity].reshape(-1, model_width)
    grads_in = got[:, capacity:].reshape(-1, model_width)
    up_local = w_up[0]
    down_local = w_down[0]
    up_full, down_full = (
        lax.all_gather(up_local, "dp", axis=0, tiled=True),
        lax.all_gather(down_local, "dp", axis=0, tiled=True),
    )
    pre = jnp.dot(inputs, up_full, preferred_element_type=jnp.float32)
    sigmoid_pre = jax.nn.sigmoid(pre)
    hidden = (pre * sigmoid_pre).astype(jnp.bfloat16)
    hidden_grad = lax.dot_general(
        grads_in, down_full, (((1,), (1,)), ((), ())), preferred_element_type=jnp.float32
    )
    pre_grad = (hidden_grad * (sigmoid_pre * (1.0 + pre * (1.0 - sigmoid_pre)))).astype(
        jnp.bfloat16
    )
    n_rows = inputs.shape[0]
    ff = hidden.shape[1]
    hidden_xy = hidden.reshape(n_rows, n_y, n_x, ff // (n_x * n_y)).transpose(0, 2, 1, 3).reshape(n_rows, ff)
    part_down = lax.dot_general(
        hidden_xy, grads_in, (((0,), (0,)), ((), ())), preferred_element_type=jnp.float32
    ).astype(jnp.bfloat16)
    part_up = lax.dot_general(
        inputs, pre_grad, (((0,), (0,)), ((), ())), preferred_element_type=jnp.float32
    ).astype(jnp.bfloat16)
    grad_up, grad_down = reduce_scatter_2d(
        part_up.reshape(n_y, n_x, -1, part_up.shape[1]),
        part_down.reshape(n_x, n_y, -1, part_down.shape[1]),
        n_x,
        n_y,
    )
    return (grad_up[None], grad_down[None])


def solution(mesh):
    n_dp = mesh.shape["dp"]
    n_x = math.isqrt(n_dp)
    n_y = n_dp // n_x
    in_specs = (
        P(("dp", "expert"), None),
        P(("dp", "expert"), None),
        P(("dp", "expert"), None),
        P(("dp", "expert"), None),
        P("expert", "dp", None),
        P("expert", "dp", None),
    )
    out_specs = (P("expert", "dp", None), P("expert", "dp", None))

    def fn(*args):
        return body(*args, n_x=n_x, n_y=n_y)

    return jax.shard_map(fn, mesh=mesh, in_specs=in_specs, out_specs=out_specs, check_vma=False)
```

```python
import math

import jax
import jax.numpy as jnp
from jax import lax
from jax.sharding import PartitionSpec as P


def slot_positions(choice_ids, capacity, experts):
    flat = choice_ids.reshape(-1)
    onehot = (flat[:, None] == jnp.arange(experts, dtype=jnp.int32)[None, :]).astype(jnp.int32)
    before = jnp.cumsum(onehot, axis=0) - onehot
    ranked = jnp.sum(before * onehot, axis=1)
    return (flat * capacity + ranked).reshape(choice_ids.shape)


def ring_perms(n_x, n_y):
    def idx(y, x):
        return y * n_x + x

    x_fwd = [(idx(y, x), idx(y, (x + 1) % n_x)) for y in range(n_y) for x in range(n_x)]
    x_bwd = [(idx(y, x), idx(y, (x - 1) % n_x)) for y in range(n_y) for x in range(n_x)]
    y_fwd = [(idx(y, x), idx((y + 1) % n_y, x)) for y in range(n_y) for x in range(n_x)]
    y_bwd = [(idx(y, x), idx((y - 1) % n_y, x)) for y in range(n_y) for x in range(n_x)]
    return {"x": (x_fwd, x_bwd), "y": (y_fwd, y_bwd)}


class RingRS:
    def __init__(self, chunks, pos, n, perms):
        h = chunks.shape[1] // 2
        self.lo, self.hi = chunks[:, :h], chunks[:, h:]
        self.pos, self.n = pos, n
        self.fwd, self.bwd = perms
        self.s = 0
        self.acc_f = self.take(self.lo, (pos - 1) % n)
        self.acc_b = self.take(self.hi, (pos + 1) % n)

    @staticmethod
    def take(part, i):
        return lax.dynamic_index_in_dim(part, i, 0, keepdims=False).astype(jnp.float32)

    def step(self):
        s, pos, n = self.s, self.pos, self.n
        got_f = lax.ppermute(self.acc_f.astype(jnp.bfloat16), "dp", self.fwd)
        got_b = lax.ppermute(self.acc_b.astype(jnp.bfloat16), "dp", self.bwd)
        self.acc_f = self.take(self.lo, (pos - s - 2) % n) + got_f.astype(jnp.float32)
        self.acc_b = self.take(self.hi, (pos + s + 2) % n) + got_b.astype(jnp.float32)
        self.s += 1

    def result(self):
        return jnp.concatenate([self.acc_f, self.acc_b], axis=0)


def run_rings(ring_a, ring_b):
    while ring_a.s < ring_a.n - 1 or ring_b.s < ring_b.n - 1:
        if ring_a.s < ring_a.n - 1:
            ring_a.step()
        if ring_b.s < ring_b.n - 1:
            ring_b.step()
    return ring_a.result(), ring_b.result()


def reduce_scatter_2d(part_up, part_down_xy, n_x, n_y):
    dp = lax.axis_index("dp")
    px, py = dp % n_x, dp // n_x
    perms = ring_perms(n_x, n_y)
    up1, down1 = run_rings(
        RingRS(part_up, py, n_y, perms["y"]), RingRS(part_down_xy, px, n_x, perms["x"])
    )
    return run_rings(RingRS(up1, px, n_x, perms["x"]), RingRS(down1, py, n_y, perms["y"]))


def body(tokens, cotangent, probs, expert_ids, w_up, w_down, n_x, n_y):
    tok_count, model_width = tokens.shape
    experts = lax.axis_size("expert")
    capacity = 2 * tok_count // experts + 1
    slot_of = slot_positions(expert_ids, capacity, experts)
    slot_ids = jnp.arange(experts * capacity, dtype=jnp.int32)
    matches = slot_ids[:, None, None] == slot_of[None, :, :]
    placing = jnp.any(matches, axis=2).astype(jnp.bfloat16)
    factor = jnp.sum(jnp.where(matches, probs[None, :, :], jnp.float32(0.0)), axis=(1, 2))
    x_slots = jnp.dot(placing, tokens, preferred_element_type=jnp.float32).astype(jnp.bfloat16)
    cot_slots = jnp.dot(placing, cotangent, preferred_element_type=jnp.float32)
    scaled = (cot_slots * factor[:, None]).astype(jnp.bfloat16)
    per_expert = capacity * model_width
    lanes = 128 if per_expert % 128 == 0 else model_width
    wire_shape = (experts, per_expert // lanes, lanes)
    got_inputs = lax.all_to_all(
        x_slots.reshape(wire_shape), "expert", split_axis=0, concat_axis=0, tiled=True
    )
    got_grads = lax.all_to_all(
        scaled.reshape(wire_shape), "expert", split_axis=0, concat_axis=0, tiled=True
    )
    inputs = got_inputs.reshape(-1, model_width)
    grads_in = got_grads.reshape(-1, model_width)
    up_local = w_up[0]
    down_local = w_down[0]
    up_full, down_full = (
        lax.all_gather(up_local, "dp", axis=0, tiled=True),
        lax.all_gather(down_local, "dp", axis=0, tiled=True),
    )
    pre = jnp.dot(inputs, up_full, preferred_element_type=jnp.float32)
    sigmoid_pre = jax.nn.sigmoid(pre)
    hidden = (pre * sigmoid_pre).astype(jnp.bfloat16)
    hidden_grad = lax.dot_general(
        grads_in, down_full, (((1,), (1,)), ((), ())), preferred_element_type=jnp.float32
    )
    pre_grad = (hidden_grad * (sigmoid_pre * (1.0 + pre * (1.0 - sigmoid_pre)))).astype(
        jnp.bfloat16
    )
    n_rows = inputs.shape[0]
    ff = hidden.shape[1]
    hidden_xy = hidden.reshape(n_rows, n_y, n_x, ff // (n_x * n_y)).transpose(0, 2, 1, 3).reshape(n_rows, ff)
    part_down = lax.dot_general(
        hidden_xy, grads_in, (((0,), (0,)), ((), ())), preferred_element_type=jnp.float32
    ).astype(jnp.bfloat16)
    part_up = lax.dot_general(
        inputs, pre_grad, (((0,), (0,)), ((), ())), preferred_element_type=jnp.float32
    ).astype(jnp.bfloat16)
    grad_up, grad_down = reduce_scatter_2d(
        part_up.reshape(n_y, n_x, -1, part_up.shape[1]),
        part_down.reshape(n_x, n_y, -1, part_down.shape[1]),
        n_x,
        n_y,
    )
    return (grad_up[None], grad_down[None])


def solution(mesh):
    n_dp = mesh.shape["dp"]
    n_x = math.isqrt(n_dp)
    n_y = n_dp // n_x
    in_specs = (
        P(("dp", "expert"), None),
        P(("dp", "expert"), None),
        P(("dp", "expert"), None),
        P(("dp", "expert"), None),
        P("expert", "dp", None),
        P("expert", "dp", None),
    )
    out_specs = (P("expert", "dp", None), P("expert", "dp", None))

    def fn(*args):
        return body(*args, n_x=n_x, n_y=n_y)

    return jax.shard_map(fn, mesh=mesh, in_specs=in_specs, out_specs=out_specs, check_vma=False)
```

```python
import math

import jax
import jax.numpy as jnp
from jax import lax
from jax.sharding import PartitionSpec as P


def slot_positions(choice_ids, capacity, experts):
    flat = choice_ids.reshape(-1)
    onehot = (flat[:, None] == jnp.arange(experts, dtype=jnp.int32)[None, :]).astype(jnp.int32)
    before = jnp.cumsum(onehot, axis=0) - onehot
    ranked = jnp.sum(before * onehot, axis=1)
    return (flat * capacity + ranked).reshape(choice_ids.shape)


def ring_perms(n_x, n_y):
    def idx(y, x):
        return y * n_x + x

    x_fwd = [(idx(y, x), idx(y, (x + 1) % n_x)) for y in range(n_y) for x in range(n_x)]
    x_bwd = [(idx(y, x), idx(y, (x - 1) % n_x)) for y in range(n_y) for x in range(n_x)]
    y_fwd = [(idx(y, x), idx((y + 1) % n_y, x)) for y in range(n_y) for x in range(n_x)]
    y_bwd = [(idx(y, x), idx((y - 1) % n_y, x)) for y in range(n_y) for x in range(n_x)]
    return {"x": (x_fwd, x_bwd), "y": (y_fwd, y_bwd)}


class RingRS:
    def __init__(self, chunks, pos, n, perms):
        h = chunks.shape[1] // 2
        self.lo, self.hi = chunks[:, :h], chunks[:, h:]
        self.pos, self.n = pos, n
        self.fwd, self.bwd = perms
        self.s = 0
        self.acc_f = self.take(self.lo, (pos - 1) % n)
        self.acc_b = self.take(self.hi, (pos + 1) % n)

    @staticmethod
    def take(part, i):
        return lax.dynamic_index_in_dim(part, i, 0, keepdims=False).astype(jnp.float32)

    def step(self):
        s, pos, n = self.s, self.pos, self.n
        got_f = lax.ppermute(self.acc_f.astype(jnp.bfloat16), "dp", self.fwd)
        got_b = lax.ppermute(self.acc_b.astype(jnp.bfloat16), "dp", self.bwd)
        self.acc_f = self.take(self.lo, (pos - s - 2) % n) + got_f.astype(jnp.float32)
        self.acc_b = self.take(self.hi, (pos + s + 2) % n) + got_b.astype(jnp.float32)
        self.s += 1

    def result(self):
        return jnp.concatenate([self.acc_f, self.acc_b], axis=0)


def run_rings(ring_a, ring_b):
    while ring_a.s < ring_a.n - 1 or ring_b.s < ring_b.n - 1:
        if ring_a.s < ring_a.n - 1:
            ring_a.step()
        if ring_b.s < ring_b.n - 1:
            ring_b.step()
    return ring_a.result(), ring_b.result()


def reduce_scatter_2d(part_yx, part_xy, n_x, n_y):
    dp = lax.axis_index("dp")
    px, py = dp % n_x, dp // n_x
    perms = ring_perms(n_x, n_y)
    yx1, xy1 = run_rings(
        RingRS(part_yx, py, n_y, perms["y"]), RingRS(part_xy, px, n_x, perms["x"])
    )
    return run_rings(RingRS(yx1, px, n_x, perms["x"]), RingRS(xy1, py, n_y, perms["y"]))


def body(tokens, cotangent, probs, expert_ids, w_up, w_down, n_x, n_y):
    tok_count, model_width = tokens.shape
    experts = lax.axis_size("expert")
    capacity = 2 * tok_count // experts + 1
    slot_of = slot_positions(expert_ids, capacity, experts)
    slot_ids = jnp.arange(experts * capacity, dtype=jnp.int32)
    matches = slot_ids[:, None, None] == slot_of[None, :, :]
    placing = jnp.any(matches, axis=2).astype(jnp.bfloat16)
    factor = jnp.sum(jnp.where(matches, probs[None, :, :], jnp.float32(0.0)), axis=(1, 2))
    x_slots = jnp.dot(placing, tokens, preferred_element_type=jnp.float32).astype(jnp.bfloat16)
    cot_slots = jnp.dot(placing, cotangent, preferred_element_type=jnp.float32)
    scaled = (cot_slots * factor[:, None]).astype(jnp.bfloat16)
    per_expert = capacity * model_width
    lanes = 128 if per_expert % 128 == 0 else model_width
    wire_shape = (experts, per_expert // lanes, lanes)
    got_inputs = lax.all_to_all(
        x_slots.reshape(wire_shape), "expert", split_axis=0, concat_axis=0, tiled=True
    )
    got_grads = lax.all_to_all(
        scaled.reshape(wire_shape), "expert", split_axis=0, concat_axis=0, tiled=True
    )
    inputs = got_inputs.reshape(-1, model_width)
    grads_in = got_grads.reshape(-1, model_width)
    up_local = w_up[0]
    down_local = w_down[0]
    up_full, down_full = (
        lax.all_gather(up_local, "dp", axis=0, tiled=True),
        lax.all_gather(down_local, "dp", axis=0, tiled=True),
    )
    pre = jnp.dot(inputs, up_full, preferred_element_type=jnp.float32)
    sigmoid_pre = jax.nn.sigmoid(pre)
    hidden = (pre * sigmoid_pre).astype(jnp.bfloat16)
    hidden_grad = lax.dot_general(
        grads_in, down_full, (((1,), (1,)), ((), ())), preferred_element_type=jnp.float32
    )
    pre_grad = (hidden_grad * (sigmoid_pre * (1.0 + pre * (1.0 - sigmoid_pre)))).astype(
        jnp.bfloat16
    )
    n_rows = inputs.shape[0]
    ff = hidden.shape[1]
    half = model_width // 2
    hidden_xy = hidden.reshape(n_rows, n_y, n_x, ff // (n_x * n_y)).transpose(0, 2, 1, 3).reshape(n_rows, ff)
    down_xy = lax.dot_general(
        hidden_xy, grads_in[:, :half], (((0,), (0,)), ((), ())), preferred_element_type=jnp.float32
    ).astype(jnp.bfloat16)
    down_yx = lax.dot_general(
        hidden, grads_in[:, half:], (((0,), (0,)), ((), ())), preferred_element_type=jnp.float32
    ).astype(jnp.bfloat16)
    part_up = lax.dot_general(
        inputs, pre_grad, (((0,), (0,)), ((), ())), preferred_element_type=jnp.float32
    ).astype(jnp.bfloat16)
    grad_up = lax.psum_scatter(part_up, "dp", scatter_dimension=0, tiled=True).astype(jnp.float32)
    left, right = reduce_scatter_2d(
        down_yx.reshape(n_y, n_x, -1, half),
        down_xy.reshape(n_x, n_y, -1, half),
        n_x,
        n_y,
    )
    grad_down = jnp.concatenate([right, left], axis=1)
    return (grad_up[None], grad_down[None])


def solution(mesh):
    n_dp = mesh.shape["dp"]
    n_x = math.isqrt(n_dp)
    n_y = n_dp // n_x
    in_specs = (
        P(("dp", "expert"), None),
        P(("dp", "expert"), None),
        P(("dp", "expert"), None),
        P(("dp", "expert"), None),
        P("expert", "dp", None),
        P("expert", "dp", None),
    )
    out_specs = (P("expert", "dp", None), P("expert", "dp", None))

    def fn(*args):
        return body(*args, n_x=n_x, n_y=n_y)

    return jax.shard_map(fn, mesh=mesh, in_specs=in_specs, out_specs=out_specs, check_vma=False)
```

```python
import math

import jax
import jax.numpy as jnp
from jax import lax
from jax.sharding import PartitionSpec as P


def slot_positions(choice_ids, capacity, experts):
    flat = choice_ids.reshape(-1)
    onehot = (flat[:, None] == jnp.arange(experts, dtype=jnp.int32)[None, :]).astype(jnp.int32)
    before = jnp.cumsum(onehot, axis=0) - onehot
    ranked = jnp.sum(before * onehot, axis=1)
    return (flat * capacity + ranked).reshape(choice_ids.shape)


def shift_perms(n_x, n_y, axis, k):
    if axis == "x":
        return [(y * n_x + x, y * n_x + (x + k) % n_x) for y in range(n_y) for x in range(n_x)]
    return [(y * n_x + x, ((y + k) % n_y) * n_x + x) for y in range(n_y) for x in range(n_x)]


def direct_rs(chunks, pos, n, axis, n_x, n_y):
    total = lax.dynamic_index_in_dim(chunks, pos, 0, keepdims=False).astype(jnp.float32)
    for k in range(1, n):
        sent = lax.dynamic_index_in_dim(chunks, (pos + k) % n, 0, keepdims=False)
        got = lax.ppermute(sent.astype(jnp.bfloat16), "dp", shift_perms(n_x, n_y, axis, k))
        total = total + got.astype(jnp.float32)
    return total


def ring_perms(n_x, n_y):
    def idx(y, x):
        return y * n_x + x

    x_fwd = [(idx(y, x), idx(y, (x + 1) % n_x)) for y in range(n_y) for x in range(n_x)]
    x_bwd = [(idx(y, x), idx(y, (x - 1) % n_x)) for y in range(n_y) for x in range(n_x)]
    y_fwd = [(idx(y, x), idx((y + 1) % n_y, x)) for y in range(n_y) for x in range(n_x)]
    y_bwd = [(idx(y, x), idx((y - 1) % n_y, x)) for y in range(n_y) for x in range(n_x)]
    return {"x": (x_fwd, x_bwd), "y": (y_fwd, y_bwd)}


class RingRS:
    def __init__(self, chunks, pos, n, perms):
        h = chunks.shape[1] // 2
        self.lo, self.hi = chunks[:, :h], chunks[:, h:]
        self.pos, self.n = pos, n
        self.fwd, self.bwd = perms
        self.s = 0
        self.acc_f = self.take(self.lo, (pos - 1) % n)
        self.acc_b = self.take(self.hi, (pos + 1) % n)

    @staticmethod
    def take(part, i):
        return lax.dynamic_index_in_dim(part, i, 0, keepdims=False).astype(jnp.float32)

    def step(self):
        s, pos, n = self.s, self.pos, self.n
        got_f = lax.ppermute(self.acc_f.astype(jnp.bfloat16), "dp", self.fwd)
        got_b = lax.ppermute(self.acc_b.astype(jnp.bfloat16), "dp", self.bwd)
        self.acc_f = self.take(self.lo, (pos - s - 2) % n) + got_f.astype(jnp.float32)
        self.acc_b = self.take(self.hi, (pos + s + 2) % n) + got_b.astype(jnp.float32)
        self.s += 1

    def result(self):
        return jnp.concatenate([self.acc_f, self.acc_b], axis=0)


def run_rings(ring_a, ring_b):
    while ring_a.s < ring_a.n - 1 or ring_b.s < ring_b.n - 1:
        if ring_a.s < ring_a.n - 1:
            ring_a.step()
        if ring_b.s < ring_b.n - 1:
            ring_b.step()
    return ring_a.result(), ring_b.result()


def reduce_scatter_2d(part_yx, part_xy, n_x, n_y):
    dp = lax.axis_index("dp")
    px, py = dp % n_x, dp // n_x
    perms = ring_perms(n_x, n_y)
    yx1, xy1 = run_rings(
        RingRS(part_yx, py, n_y, perms["y"]), RingRS(part_xy, px, n_x, perms["x"])
    )
    return direct_rs(yx1, px, n_x, "x", n_x, n_y), direct_rs(xy1, py, n_y, "y", n_x, n_y)


def body(tokens, cotangent, probs, expert_ids, w_up, w_down, n_x, n_y):
    tok_count, model_width = tokens.shape
    experts = lax.axis_size("expert")
    capacity = 2 * tok_count // experts + 1
    slot_of = slot_positions(expert_ids, capacity, experts)
    slot_ids = jnp.arange(experts * capacity, dtype=jnp.int32)
    matches = slot_ids[:, None, None] == slot_of[None, :, :]
    placing = jnp.any(matches, axis=2).astype(jnp.bfloat16)
    factor = jnp.sum(jnp.where(matches, probs[None, :, :], jnp.float32(0.0)), axis=(1, 2))
    x_slots = jnp.dot(placing, tokens, preferred_element_type=jnp.float32).astype(jnp.bfloat16)
    cot_slots = jnp.dot(placing, cotangent, preferred_element_type=jnp.float32)
    scaled = (cot_slots * factor[:, None]).astype(jnp.bfloat16)
    per_expert = capacity * model_width
    lanes = 128 if per_expert % 128 == 0 else model_width
    wire_shape = (experts, per_expert // lanes, lanes)
    got_inputs = lax.all_to_all(
        x_slots.reshape(wire_shape), "expert", split_axis=0, concat_axis=0, tiled=True
    )
    got_grads = lax.all_to_all(
        scaled.reshape(wire_shape), "expert", split_axis=0, concat_axis=0, tiled=True
    )
    inputs = got_inputs.reshape(-1, model_width)
    grads_in = got_grads.reshape(-1, model_width)
    up_local = w_up[0]
    down_local = w_down[0]
    up_full, down_full = (
        lax.all_gather(up_local, "dp", axis=0, tiled=True),
        lax.all_gather(down_local, "dp", axis=0, tiled=True),
    )
    pre = jnp.dot(inputs, up_full, preferred_element_type=jnp.float32)
    sigmoid_pre = jax.nn.sigmoid(pre)
    hidden = (pre * sigmoid_pre).astype(jnp.bfloat16)
    hidden_grad = lax.dot_general(
        grads_in, down_full, (((1,), (1,)), ((), ())), preferred_element_type=jnp.float32
    )
    pre_grad = (hidden_grad * (sigmoid_pre * (1.0 + pre * (1.0 - sigmoid_pre)))).astype(
        jnp.bfloat16
    )
    n_rows = inputs.shape[0]
    ff = hidden.shape[1]
    half = model_width // 2
    part_up = lax.dot_general(
        inputs, pre_grad, (((0,), (0,)), ((), ())), preferred_element_type=jnp.float32
    ).astype(jnp.bfloat16)
    grad_up = lax.psum_scatter(part_up, "dp", scatter_dimension=0, tiled=True).astype(jnp.float32)
    _, hidden = lax.optimization_barrier((part_up, hidden))
    hidden_xy = hidden.reshape(n_rows, n_y, n_x, ff // (n_x * n_y)).transpose(0, 2, 1, 3).reshape(n_rows, ff)
    down_xy = lax.dot_general(
        hidden_xy, grads_in[:, :half], (((0,), (0,)), ((), ())), preferred_element_type=jnp.float32
    ).astype(jnp.bfloat16)
    down_yx = lax.dot_general(
        hidden, grads_in[:, half:], (((0,), (0,)), ((), ())), preferred_element_type=jnp.float32
    ).astype(jnp.bfloat16)
    left, right = reduce_scatter_2d(
        down_yx.reshape(n_y, n_x, -1, half),
        down_xy.reshape(n_x, n_y, -1, half),
        n_x,
        n_y,
    )
    grad_down = jnp.concatenate([right, left], axis=1)
    return (grad_up[None], grad_down[None])


def solution(mesh):
    n_dp = mesh.shape["dp"]
    n_x = math.isqrt(n_dp)
    n_y = n_dp // n_x
    in_specs = (
        P(("dp", "expert"), None),
        P(("dp", "expert"), None),
        P(("dp", "expert"), None),
        P(("dp", "expert"), None),
        P("expert", "dp", None),
        P("expert", "dp", None),
    )
    out_specs = (P("expert", "dp", None), P("expert", "dp", None))

    def fn(*args):
        return body(*args, n_x=n_x, n_y=n_y)

    return jax.shard_map(fn, mesh=mesh, in_specs=in_specs, out_specs=out_specs, check_vma=False)
```

```python
import math

import jax
import jax.numpy as jnp
from jax import lax
from jax.sharding import PartitionSpec as P


def slot_positions(choice_ids, capacity, experts):
    flat = choice_ids.reshape(-1)
    onehot = (flat[:, None] == jnp.arange(experts, dtype=jnp.int32)[None, :]).astype(jnp.int32)
    before = jnp.cumsum(onehot, axis=0) - onehot
    ranked = jnp.sum(before * onehot, axis=1)
    return (flat * capacity + ranked).reshape(choice_ids.shape)


def shift_perms(n_x, n_y, axis, k):
    if axis == "x":
        return [(y * n_x + x, y * n_x + (x + k) % n_x) for y in range(n_y) for x in range(n_x)]
    return [(y * n_x + x, ((y + k) % n_y) * n_x + x) for y in range(n_y) for x in range(n_x)]


def direct_rs(chunks, pos, n, axis, n_x, n_y):
    total = lax.dynamic_index_in_dim(chunks, pos, 0, keepdims=False).astype(jnp.float32)
    for k in range(1, n):
        sent = lax.dynamic_index_in_dim(chunks, (pos + k) % n, 0, keepdims=False)
        got = lax.ppermute(sent.astype(jnp.bfloat16), "dp", shift_perms(n_x, n_y, axis, k))
        total = total + got.astype(jnp.float32)
    return total


def ring_perms(n_x, n_y):
    def idx(y, x):
        return y * n_x + x

    x_fwd = [(idx(y, x), idx(y, (x + 1) % n_x)) for y in range(n_y) for x in range(n_x)]
    x_bwd = [(idx(y, x), idx(y, (x - 1) % n_x)) for y in range(n_y) for x in range(n_x)]
    y_fwd = [(idx(y, x), idx((y + 1) % n_y, x)) for y in range(n_y) for x in range(n_x)]
    y_bwd = [(idx(y, x), idx((y - 1) % n_y, x)) for y in range(n_y) for x in range(n_x)]
    return {"x": (x_fwd, x_bwd), "y": (y_fwd, y_bwd)}


class RingRS:
    def __init__(self, chunks, pos, n, perms):
        h = chunks.shape[1] // 2
        self.lo, self.hi = chunks[:, :h], chunks[:, h:]
        self.pos, self.n = pos, n
        self.fwd, self.bwd = perms
        self.s = 0
        self.acc_f = self.take(self.lo, (pos - 1) % n)
        self.acc_b = self.take(self.hi, (pos + 1) % n)

    @staticmethod
    def take(part, i):
        return lax.dynamic_index_in_dim(part, i, 0, keepdims=False).astype(jnp.float32)

    def step(self):
        s, pos, n = self.s, self.pos, self.n
        got_f = lax.ppermute(self.acc_f.astype(jnp.bfloat16), "dp", self.fwd)
        got_b = lax.ppermute(self.acc_b.astype(jnp.bfloat16), "dp", self.bwd)
        self.acc_f = self.take(self.lo, (pos - s - 2) % n) + got_f.astype(jnp.float32)
        self.acc_b = self.take(self.hi, (pos + s + 2) % n) + got_b.astype(jnp.float32)
        self.s += 1

    def result(self):
        return jnp.concatenate([self.acc_f, self.acc_b], axis=0)


def run_rings(ring_a, ring_b):
    while ring_a.s < ring_a.n - 1 or ring_b.s < ring_b.n - 1:
        if ring_a.s < ring_a.n - 1:
            ring_a.step()
        if ring_b.s < ring_b.n - 1:
            ring_b.step()
    return ring_a.result(), ring_b.result()


def reduce_scatter_2d(part_yx, part_xy, n_x, n_y):
    dp = lax.axis_index("dp")
    px, py = dp % n_x, dp // n_x
    perms = ring_perms(n_x, n_y)
    yx1, xy1 = run_rings(
        RingRS(part_yx, py, n_y, perms["y"]), RingRS(part_xy, px, n_x, perms["x"])
    )
    return direct_rs(yx1, px, n_x, "x", n_x, n_y), direct_rs(xy1, py, n_y, "y", n_x, n_y)


def body(tokens, cotangent, probs, expert_ids, w_up, w_down, n_x, n_y):
    tok_count, model_width = tokens.shape
    experts = lax.axis_size("expert")
    capacity = 2 * tok_count // experts + 1
    slot_of = slot_positions(expert_ids, capacity, experts)
    slot_ids = jnp.arange(experts * capacity, dtype=jnp.int32)
    matches = slot_ids[:, None, None] == slot_of[None, :, :]
    placing = jnp.any(matches, axis=2).astype(jnp.bfloat16)
    factor = jnp.sum(jnp.where(matches, probs[None, :, :], jnp.float32(0.0)), axis=(1, 2))
    x_slots = jnp.dot(placing, tokens, preferred_element_type=jnp.float32).astype(jnp.bfloat16)
    cot_slots = jnp.dot(placing, cotangent, preferred_element_type=jnp.float32)
    scaled = (cot_slots * factor[:, None]).astype(jnp.bfloat16)
    per_expert = capacity * model_width
    lanes = 128 if per_expert % 128 == 0 else model_width
    wire_shape = (experts, per_expert // lanes, lanes)
    got_inputs = lax.all_to_all(
        x_slots.reshape(wire_shape), "expert", split_axis=0, concat_axis=0, tiled=True
    )
    got_grads = lax.all_to_all(
        scaled.reshape(wire_shape), "expert", split_axis=0, concat_axis=0, tiled=True
    )
    inputs = got_inputs.reshape(-1, model_width)
    grads_in = got_grads.reshape(-1, model_width)
    up_local = w_up[0]
    down_local = w_down[0]
    up_full, down_full = (
        lax.all_gather(up_local, "dp", axis=0, tiled=True),
        lax.all_gather(down_local, "dp", axis=0, tiled=True),
    )
    ff = up_full.shape[-1]
    n_rows = inputs.shape[0]
    half = model_width // 2
    x_rows, g_rows = inputs, grads_in
    hiddens, ups = [], []
    for part in range(2):
        cols = slice(part * ff // 2, (part + 1) * ff // 2)
        pre = jnp.dot(x_rows, up_full[:, cols], preferred_element_type=jnp.float32)
        sigmoid_pre = jax.nn.sigmoid(pre)
        hiddens.append((pre * sigmoid_pre).astype(jnp.bfloat16))
        hidden_grad = lax.dot_general(
            g_rows, down_full[cols], (((1,), (1,)), ((), ())), preferred_element_type=jnp.float32
        )
        pre_grad = (hidden_grad * (sigmoid_pre * (1.0 + pre * (1.0 - sigmoid_pre)))).astype(
            jnp.bfloat16
        )
        part_up = lax.dot_general(
            x_rows, pre_grad, (((0,), (0,)), ((), ())), preferred_element_type=jnp.float32
        ).astype(jnp.bfloat16)
        ups.append(lax.psum_scatter(part_up, "dp", scatter_dimension=0, tiled=True))
        part_up, x_rows, g_rows = lax.optimization_barrier((part_up, x_rows, g_rows))
    grad_up = jnp.concatenate(ups, axis=1).astype(jnp.float32)
    hidden = jnp.concatenate(hiddens, axis=1)
    _, hidden = lax.optimization_barrier((part_up, hidden))
    hidden_xy = hidden.reshape(n_rows, n_y, n_x, ff // (n_x * n_y)).transpose(0, 2, 1, 3).reshape(n_rows, ff)
    down_xy = lax.dot_general(
        hidden_xy, grads_in[:, :half], (((0,), (0,)), ((), ())), preferred_element_type=jnp.float32
    ).astype(jnp.bfloat16)
    down_yx = lax.dot_general(
        hidden, grads_in[:, half:], (((0,), (0,)), ((), ())), preferred_element_type=jnp.float32
    ).astype(jnp.bfloat16)
    left, right = reduce_scatter_2d(
        down_yx.reshape(n_y, n_x, -1, half),
        down_xy.reshape(n_x, n_y, -1, half),
        n_x,
        n_y,
    )
    grad_down = jnp.concatenate([right, left], axis=1)
    return (grad_up[None], grad_down[None])


def solution(mesh):
    n_dp = mesh.shape["dp"]
    n_x = math.isqrt(n_dp)
    n_y = n_dp // n_x
    in_specs = (
        P(("dp", "expert"), None),
        P(("dp", "expert"), None),
        P(("dp", "expert"), None),
        P(("dp", "expert"), None),
        P("expert", "dp", None),
        P("expert", "dp", None),
    )
    out_specs = (P("expert", "dp", None), P("expert", "dp", None))

    def fn(*args):
        return body(*args, n_x=n_x, n_y=n_y)

    return jax.shard_map(fn, mesh=mesh, in_specs=in_specs, out_specs=out_specs, check_vma=False)
```

```python
import math

import jax
import jax.numpy as jnp
from jax import lax
from jax.sharding import PartitionSpec as P


def slot_positions(choice_ids, capacity, experts):
    flat = choice_ids.reshape(-1)
    onehot = (flat[:, None] == jnp.arange(experts, dtype=jnp.int32)[None, :]).astype(jnp.int32)
    before = jnp.cumsum(onehot, axis=0) - onehot
    ranked = jnp.sum(before * onehot, axis=1)
    return (flat * capacity + ranked).reshape(choice_ids.shape)


def shift_perms(n_x, n_y, axis, k):
    if axis == "x":
        return [(y * n_x + x, y * n_x + (x + k) % n_x) for y in range(n_y) for x in range(n_x)]
    return [(y * n_x + x, ((y + k) % n_y) * n_x + x) for y in range(n_y) for x in range(n_x)]


def direct_rs(chunks, pos, n, axis, n_x, n_y):
    total = lax.dynamic_index_in_dim(chunks, pos, 0, keepdims=False).astype(jnp.float32)
    for k in range(1, n):
        sent = lax.dynamic_index_in_dim(chunks, (pos + k) % n, 0, keepdims=False)
        got = lax.ppermute(sent.astype(jnp.bfloat16), "dp", shift_perms(n_x, n_y, axis, k))
        total = total + got.astype(jnp.float32)
    return total


def ring_perms(n_x, n_y):
    def idx(y, x):
        return y * n_x + x

    x_fwd = [(idx(y, x), idx(y, (x + 1) % n_x)) for y in range(n_y) for x in range(n_x)]
    x_bwd = [(idx(y, x), idx(y, (x - 1) % n_x)) for y in range(n_y) for x in range(n_x)]
    y_fwd = [(idx(y, x), idx((y + 1) % n_y, x)) for y in range(n_y) for x in range(n_x)]
    y_bwd = [(idx(y, x), idx((y - 1) % n_y, x)) for y in range(n_y) for x in range(n_x)]
    return {"x": (x_fwd, x_bwd), "y": (y_fwd, y_bwd)}


class RingRS:
    def __init__(self, chunks, pos, n, perms):
        h = chunks.shape[1] // 2
        self.lo, self.hi = chunks[:, :h], chunks[:, h:]
        self.pos, self.n = pos, n
        self.fwd, self.bwd = perms
        self.s = 0
        self.acc_f = self.take(self.lo, (pos - 1) % n)
        self.acc_b = self.take(self.hi, (pos + 1) % n)

    @staticmethod
    def take(part, i):
        return lax.dynamic_index_in_dim(part, i, 0, keepdims=False).astype(jnp.float32)

    def step(self):
        s, pos, n = self.s, self.pos, self.n
        got_f = lax.ppermute(self.acc_f.astype(jnp.bfloat16), "dp", self.fwd)
        got_b = lax.ppermute(self.acc_b.astype(jnp.bfloat16), "dp", self.bwd)
        self.acc_f = self.take(self.lo, (pos - s - 2) % n) + got_f.astype(jnp.float32)
        self.acc_b = self.take(self.hi, (pos + s + 2) % n) + got_b.astype(jnp.float32)
        self.s += 1

    def result(self):
        return jnp.concatenate([self.acc_f, self.acc_b], axis=0)


def run_rings(ring_a, ring_b):
    while ring_a.s < ring_a.n - 1 or ring_b.s < ring_b.n - 1:
        if ring_a.s < ring_a.n - 1:
            ring_a.step()
        if ring_b.s < ring_b.n - 1:
            ring_b.step()
    return ring_a.result(), ring_b.result()


def reduce_scatter_2d(part_yx, part_xy, n_x, n_y):
    dp = lax.axis_index("dp")
    px, py = dp % n_x, dp // n_x
    perms = ring_perms(n_x, n_y)
    yx1, xy1 = run_rings(
        RingRS(part_yx, py, n_y, perms["y"]), RingRS(part_xy, px, n_x, perms["x"])
    )
    return direct_rs(yx1, px, n_x, "x", n_x, n_y), direct_rs(xy1, py, n_y, "y", n_x, n_y)


def body(tokens, cotangent, probs, expert_ids, w_up, w_down, n_x, n_y):
    tok_count, model_width = tokens.shape
    experts = lax.axis_size("expert")
    capacity = 2 * tok_count // experts + 1
    slot_of = slot_positions(expert_ids, capacity, experts)
    slot_ids = jnp.arange(experts * capacity, dtype=jnp.int32)
    matches = slot_ids[:, None, None] == slot_of[None, :, :]
    placing = jnp.any(matches, axis=2).astype(jnp.bfloat16)
    factor = jnp.sum(jnp.where(matches, probs[None, :, :], jnp.float32(0.0)), axis=(1, 2))
    x_slots = jnp.dot(placing, tokens, preferred_element_type=jnp.float32).astype(jnp.bfloat16)
    cot_slots = jnp.dot(placing, cotangent, preferred_element_type=jnp.float32)
    scaled = (cot_slots * factor[:, None]).astype(jnp.bfloat16)
    per_expert = capacity * model_width
    lanes = 128 if per_expert % 128 == 0 else model_width
    wire_shape = (experts, per_expert // lanes, lanes)
    got_inputs = lax.all_to_all(
        x_slots.reshape(wire_shape), "expert", split_axis=0, concat_axis=0, tiled=True
    )
    got_grads = lax.all_to_all(
        scaled.reshape(wire_shape), "expert", split_axis=0, concat_axis=0, tiled=True
    )
    inputs = got_inputs.reshape(-1, model_width)
    grads_in = got_grads.reshape(-1, model_width)
    up_local = w_up[0]
    down_local = w_down[0]
    up_full, down_full = (
        lax.all_gather(up_local, "dp", axis=0, tiled=True),
        lax.all_gather(down_local, "dp", axis=0, tiled=True),
    )
    pre = jnp.dot(inputs, up_full, preferred_element_type=jnp.float32)
    sigmoid_pre = jax.nn.sigmoid(pre)
    hidden = (pre * sigmoid_pre).astype(jnp.bfloat16)
    n_rows = inputs.shape[0]
    ff = hidden.shape[1]
    part_down = lax.dot_general(
        hidden, grads_in, (((0,), (0,)), ((), ())), preferred_element_type=jnp.float32
    ).astype(jnp.bfloat16)
    grad_down = lax.psum_scatter(part_down, "dp", scatter_dimension=0, tiled=True).astype(jnp.float32)
    _, g_rows = lax.optimization_barrier((part_down, grads_in))
    hidden_grad = lax.dot_general(
        g_rows, down_full, (((1,), (1,)), ((), ())), preferred_element_type=jnp.float32
    )
    pre_grad = (hidden_grad * (sigmoid_pre * (1.0 + pre * (1.0 - sigmoid_pre)))).astype(
        jnp.bfloat16
    )
    half = ff // 2
    inputs_xy = inputs.reshape(n_rows, n_y, n_x, model_width // (n_x * n_y)).transpose(0, 2, 1, 3)
    inputs_xy = inputs_xy.reshape(n_rows, model_width)
    up_yx = lax.dot_general(
        inputs, pre_grad[:, :half], (((0,), (0,)), ((), ())), preferred_element_type=jnp.float32
    ).astype(jnp.bfloat16)
    up_xy = lax.dot_general(
        inputs_xy, pre_grad[:, half:], (((0,), (0,)), ((), ())), preferred_element_type=jnp.float32
    ).astype(jnp.bfloat16)
    left, right = reduce_scatter_2d(
        up_yx.reshape(n_y, n_x, -1, half),
        up_xy.reshape(n_x, n_y, -1, half),
        n_x,
        n_y,
    )
    grad_up = jnp.concatenate([left, right], axis=1)
    return (grad_up[None], grad_down[None])


def solution(mesh):
    n_dp = mesh.shape["dp"]
    n_x = math.isqrt(n_dp)
    n_y = n_dp // n_x
    in_specs = (
        P(("dp", "expert"), None),
        P(("dp", "expert"), None),
        P(("dp", "expert"), None),
        P(("dp", "expert"), None),
        P("expert", "dp", None),
        P("expert", "dp", None),
    )
    out_specs = (P("expert", "dp", None), P("expert", "dp", None))

    def fn(*args):
        return body(*args, n_x=n_x, n_y=n_y)

    return jax.shard_map(fn, mesh=mesh, in_specs=in_specs, out_specs=out_specs, check_vma=False)
```

```python
import math

import jax
import jax.numpy as jnp
from jax import lax
from jax.sharding import PartitionSpec as P


def slot_positions(choice_ids, capacity, experts):
    flat = choice_ids.reshape(-1)
    onehot = (flat[:, None] == jnp.arange(experts, dtype=jnp.int32)[None, :]).astype(jnp.int32)
    before = jnp.cumsum(onehot, axis=0) - onehot
    ranked = jnp.sum(before * onehot, axis=1)
    return (flat * capacity + ranked).reshape(choice_ids.shape)


def shift_perms(n_x, n_y, axis, k):
    if axis == "x":
        return [(y * n_x + x, y * n_x + (x + k) % n_x) for y in range(n_y) for x in range(n_x)]
    return [(y * n_x + x, ((y + k) % n_y) * n_x + x) for y in range(n_y) for x in range(n_x)]


def direct_rs(chunks, pos, n, axis, n_x, n_y):
    total = lax.dynamic_index_in_dim(chunks, pos, 0, keepdims=False).astype(jnp.float32)
    for k in range(1, n):
        sent = lax.dynamic_index_in_dim(chunks, (pos + k) % n, 0, keepdims=False)
        got = lax.ppermute(sent.astype(jnp.bfloat16), "dp", shift_perms(n_x, n_y, axis, k))
        total = total + got.astype(jnp.float32)
    return total


def ring_perms(n_x, n_y):
    def idx(y, x):
        return y * n_x + x

    x_fwd = [(idx(y, x), idx(y, (x + 1) % n_x)) for y in range(n_y) for x in range(n_x)]
    x_bwd = [(idx(y, x), idx(y, (x - 1) % n_x)) for y in range(n_y) for x in range(n_x)]
    y_fwd = [(idx(y, x), idx((y + 1) % n_y, x)) for y in range(n_y) for x in range(n_x)]
    y_bwd = [(idx(y, x), idx((y - 1) % n_y, x)) for y in range(n_y) for x in range(n_x)]
    return {"x": (x_fwd, x_bwd), "y": (y_fwd, y_bwd)}


class RingRS:
    def __init__(self, chunks, pos, n, perms):
        h = chunks.shape[1] // 2
        self.lo, self.hi = chunks[:, :h], chunks[:, h:]
        self.pos, self.n = pos, n
        self.fwd, self.bwd = perms
        self.s = 0
        self.acc_f = self.take(self.lo, (pos - 1) % n)
        self.acc_b = self.take(self.hi, (pos + 1) % n)

    @staticmethod
    def take(part, i):
        return lax.dynamic_index_in_dim(part, i, 0, keepdims=False).astype(jnp.float32)

    def step(self):
        s, pos, n = self.s, self.pos, self.n
        got_f = lax.ppermute(self.acc_f.astype(jnp.bfloat16), "dp", self.fwd)
        got_b = lax.ppermute(self.acc_b.astype(jnp.bfloat16), "dp", self.bwd)
        self.acc_f = self.take(self.lo, (pos - s - 2) % n) + got_f.astype(jnp.float32)
        self.acc_b = self.take(self.hi, (pos + s + 2) % n) + got_b.astype(jnp.float32)
        self.s += 1

    def result(self):
        return jnp.concatenate([self.acc_f, self.acc_b], axis=0)


def run_rings(ring_a, ring_b):
    while ring_a.s < ring_a.n - 1 or ring_b.s < ring_b.n - 1:
        if ring_a.s < ring_a.n - 1:
            ring_a.step()
        if ring_b.s < ring_b.n - 1:
            ring_b.step()
    return ring_a.result(), ring_b.result()


def reduce_scatter_2d(part_yx, part_xy, n_x, n_y):
    dp = lax.axis_index("dp")
    px, py = dp % n_x, dp // n_x
    perms = ring_perms(n_x, n_y)
    yx1, xy1 = run_rings(
        RingRS(part_yx, py, n_y, perms["y"]), RingRS(part_xy, px, n_x, perms["x"])
    )
    return direct_rs(yx1, px, n_x, "x", n_x, n_y), direct_rs(xy1, py, n_y, "y", n_x, n_y)


def body(tokens, cotangent, probs, expert_ids, w_up, w_down, n_x, n_y):
    tok_count, model_width = tokens.shape
    experts = lax.axis_size("expert")
    capacity = 2 * tok_count // experts + 1
    slot_of = slot_positions(expert_ids, capacity, experts)
    slot_ids = jnp.arange(experts * capacity, dtype=jnp.int32)
    matches = slot_ids[:, None, None] == slot_of[None, :, :]
    placing = jnp.any(matches, axis=2).astype(jnp.bfloat16)
    factor = jnp.sum(jnp.where(matches, probs[None, :, :], jnp.float32(0.0)), axis=(1, 2))
    x_slots = jnp.dot(placing, tokens, preferred_element_type=jnp.float32).astype(jnp.bfloat16)
    cot_slots = jnp.dot(placing, cotangent, preferred_element_type=jnp.float32)
    scaled = (cot_slots * factor[:, None]).astype(jnp.bfloat16)
    per_expert = capacity * model_width
    lanes = 128 if per_expert % 128 == 0 else model_width
    wire_shape = (experts, per_expert // lanes, lanes)
    got_inputs = lax.all_to_all(
        x_slots.reshape(wire_shape), "expert", split_axis=0, concat_axis=0, tiled=True
    )
    got_grads = lax.all_to_all(
        scaled.reshape(wire_shape), "expert", split_axis=0, concat_axis=0, tiled=True
    )
    inputs = got_inputs.reshape(-1, model_width)
    grads_in = got_grads.reshape(-1, model_width)
    up_local = w_up[0]
    down_local = w_down[0]
    up_full, down_full = (
        lax.all_gather(up_local, "dp", axis=0, tiled=True),
        lax.all_gather(down_local, "dp", axis=0, tiled=True),
    )
    pre = jnp.dot(inputs, up_full, preferred_element_type=jnp.float32)
    sigmoid_pre = jax.nn.sigmoid(pre)
    hidden = (pre * sigmoid_pre).astype(jnp.bfloat16)
    n_rows = inputs.shape[0]
    ff = hidden.shape[1]
    part_down = lax.dot_general(
        hidden, grads_in, (((0,), (0,)), ((), ())), preferred_element_type=jnp.float32
    ).astype(jnp.bfloat16)
    grad_down = lax.psum_scatter(part_down, "dp", scatter_dimension=0, tiled=True).astype(jnp.float32)
    _, g_rows = lax.optimization_barrier((part_down, grads_in))
    hidden_grad = lax.dot_general(
        g_rows, down_full, (((1,), (1,)), ((), ())), preferred_element_type=jnp.float32
    )
    pre_grad = (hidden_grad * (sigmoid_pre * (1.0 + pre * (1.0 - sigmoid_pre)))).astype(
        jnp.bfloat16
    )
    half = ff // 2
    up_yx = lax.dot_general(
        inputs, pre_grad[:, :half], (((0,), (0,)), ((), ())), preferred_element_type=jnp.float32
    ).astype(jnp.bfloat16)
    up_xy = lax.dot_general(
        inputs, pre_grad[:, half:], (((0,), (0,)), ((), ())), preferred_element_type=jnp.float32
    ).astype(jnp.bfloat16)
    up_xy = up_xy.reshape(n_y, n_x, -1, half).transpose(1, 0, 2, 3)
    left, right = reduce_scatter_2d(
        up_yx.reshape(n_y, n_x, -1, half),
        up_xy,
        n_x,
        n_y,
    )
    grad_up = jnp.concatenate([left, right], axis=1)
    return (grad_up[None], grad_down[None])


def solution(mesh):
    n_dp = mesh.shape["dp"]
    n_x = math.isqrt(n_dp)
    n_y = n_dp // n_x
    in_specs = (
        P(("dp", "expert"), None),
        P(("dp", "expert"), None),
        P(("dp", "expert"), None),
        P(("dp", "expert"), None),
        P("expert", "dp", None),
        P("expert", "dp", None),
    )
    out_specs = (P("expert", "dp", None), P("expert", "dp", None))

    def fn(*args):
        return body(*args, n_x=n_x, n_y=n_y)

    return jax.shard_map(fn, mesh=mesh, in_specs=in_specs, out_specs=out_specs, check_vma=False)
```

```python
import math

import jax
import jax.numpy as jnp
from jax import lax
from jax.sharding import PartitionSpec as P


def slot_positions(choice_ids, capacity, experts):
    flat = choice_ids.reshape(-1)
    onehot = (flat[:, None] == jnp.arange(experts, dtype=jnp.int32)[None, :]).astype(jnp.int32)
    before = jnp.cumsum(onehot, axis=0) - onehot
    ranked = jnp.sum(before * onehot, axis=1)
    return (flat * capacity + ranked).reshape(choice_ids.shape)


def shift_perms(n_x, n_y, axis, k):
    if axis == "x":
        return [(y * n_x + x, y * n_x + (x + k) % n_x) for y in range(n_y) for x in range(n_x)]
    return [(y * n_x + x, ((y + k) % n_y) * n_x + x) for y in range(n_y) for x in range(n_x)]


def direct_rs(chunks, pos, n, axis, n_x, n_y):
    total = lax.dynamic_index_in_dim(chunks, pos, 0, keepdims=False).astype(jnp.float32)
    for k in range(1, n):
        sent = lax.dynamic_index_in_dim(chunks, (pos + k) % n, 0, keepdims=False)
        got = lax.ppermute(sent.astype(jnp.bfloat16), "dp", shift_perms(n_x, n_y, axis, k))
        total = total + got.astype(jnp.float32)
    return total


def ring_perms(n_x, n_y):
    def idx(y, x):
        return y * n_x + x

    x_fwd = [(idx(y, x), idx(y, (x + 1) % n_x)) for y in range(n_y) for x in range(n_x)]
    x_bwd = [(idx(y, x), idx(y, (x - 1) % n_x)) for y in range(n_y) for x in range(n_x)]
    y_fwd = [(idx(y, x), idx((y + 1) % n_y, x)) for y in range(n_y) for x in range(n_x)]
    y_bwd = [(idx(y, x), idx((y - 1) % n_y, x)) for y in range(n_y) for x in range(n_x)]
    return {"x": (x_fwd, x_bwd), "y": (y_fwd, y_bwd)}


class RingRS:
    def __init__(self, chunks, pos, n, perms):
        h = chunks.shape[1] // 2
        self.lo, self.hi = chunks[:, :h], chunks[:, h:]
        self.pos, self.n = pos, n
        self.fwd, self.bwd = perms
        self.s = 0
        self.acc_f = self.take(self.lo, (pos - 1) % n)
        self.acc_b = self.take(self.hi, (pos + 1) % n)

    @staticmethod
    def take(part, i):
        return lax.dynamic_index_in_dim(part, i, 0, keepdims=False).astype(jnp.float32)

    def step(self):
        s, pos, n = self.s, self.pos, self.n
        got_f = lax.ppermute(self.acc_f.astype(jnp.bfloat16), "dp", self.fwd)
        got_b = lax.ppermute(self.acc_b.astype(jnp.bfloat16), "dp", self.bwd)
        self.acc_f = self.take(self.lo, (pos - s - 2) % n) + got_f.astype(jnp.float32)
        self.acc_b = self.take(self.hi, (pos + s + 2) % n) + got_b.astype(jnp.float32)
        self.s += 1

    def result(self):
        return jnp.concatenate([self.acc_f, self.acc_b], axis=0)


def run_rings(ring_a, ring_b):
    while ring_a.s < ring_a.n - 1 or ring_b.s < ring_b.n - 1:
        if ring_a.s < ring_a.n - 1:
            ring_a.step()
        if ring_b.s < ring_b.n - 1:
            ring_b.step()
    return ring_a.result(), ring_b.result()


def reduce_scatter_2d(part_yx, part_xy, n_x, n_y):
    dp = lax.axis_index("dp")
    px, py = dp % n_x, dp // n_x
    perms = ring_perms(n_x, n_y)
    yx1 = direct_rs(part_yx, py, n_y, "y", n_x, n_y)
    xy1 = direct_rs(part_xy, px, n_x, "x", n_x, n_y)
    return direct_rs(yx1, px, n_x, "x", n_x, n_y), direct_rs(xy1, py, n_y, "y", n_x, n_y)


def body(tokens, cotangent, probs, expert_ids, w_up, w_down, n_x, n_y):
    tok_count, model_width = tokens.shape
    experts = lax.axis_size("expert")
    capacity = 2 * tok_count // experts + 1
    slot_of = slot_positions(expert_ids, capacity, experts)
    slot_ids = jnp.arange(experts * capacity, dtype=jnp.int32)
    matches = slot_ids[:, None, None] == slot_of[None, :, :]
    placing = jnp.any(matches, axis=2).astype(jnp.bfloat16)
    factor = jnp.sum(jnp.where(matches, probs[None, :, :], jnp.float32(0.0)), axis=(1, 2))
    x_slots = jnp.dot(placing, tokens, preferred_element_type=jnp.float32).astype(jnp.bfloat16)
    cot_slots = jnp.dot(placing, cotangent, preferred_element_type=jnp.float32)
    scaled = (cot_slots * factor[:, None]).astype(jnp.bfloat16)
    per_expert = capacity * model_width
    lanes = 128 if per_expert % 128 == 0 else model_width
    wire_shape = (experts, per_expert // lanes, lanes)
    got_inputs = lax.all_to_all(
        x_slots.reshape(wire_shape), "expert", split_axis=0, concat_axis=0, tiled=True
    )
    got_grads = lax.all_to_all(
        scaled.reshape(wire_shape), "expert", split_axis=0, concat_axis=0, tiled=True
    )
    inputs = got_inputs.reshape(-1, model_width)
    grads_in = got_grads.reshape(-1, model_width)
    up_local = w_up[0]
    down_local = w_down[0]
    up_full, down_full = (
        lax.all_gather(up_local, "dp", axis=0, tiled=True),
        lax.all_gather(down_local, "dp", axis=0, tiled=True),
    )
    pre = jnp.dot(inputs, up_full, preferred_element_type=jnp.float32)
    sigmoid_pre = jax.nn.sigmoid(pre)
    hidden = (pre * sigmoid_pre).astype(jnp.bfloat16)
    n_rows = inputs.shape[0]
    ff = hidden.shape[1]
    part_down = lax.dot_general(
        hidden, grads_in, (((0,), (0,)), ((), ())), preferred_element_type=jnp.float32
    ).astype(jnp.bfloat16)
    grad_down = lax.psum_scatter(part_down, "dp", scatter_dimension=0, tiled=True).astype(jnp.float32)
    _, g_rows = lax.optimization_barrier((part_down, grads_in))
    hidden_grad = lax.dot_general(
        g_rows, down_full, (((1,), (1,)), ((), ())), preferred_element_type=jnp.float32
    )
    pre_grad = (hidden_grad * (sigmoid_pre * (1.0 + pre * (1.0 - sigmoid_pre)))).astype(
        jnp.bfloat16
    )
    half = ff // 2
    up_yx = lax.dot_general(
        inputs, pre_grad[:, :half], (((0,), (0,)), ((), ())), preferred_element_type=jnp.float32
    ).astype(jnp.bfloat16)
    up_xy = lax.dot_general(
        inputs, pre_grad[:, half:], (((0,), (0,)), ((), ())), preferred_element_type=jnp.float32
    ).astype(jnp.bfloat16)
    up_xy = up_xy.reshape(n_y, n_x, -1, half).transpose(1, 0, 2, 3)
    left, right = reduce_scatter_2d(
        up_yx.reshape(n_y, n_x, -1, half),
        up_xy,
        n_x,
        n_y,
    )
    grad_up = jnp.concatenate([left, right], axis=1)
    return (grad_up[None], grad_down[None])


def solution(mesh):
    n_dp = mesh.shape["dp"]
    n_x = math.isqrt(n_dp)
    n_y = n_dp // n_x
    in_specs = (
        P(("dp", "expert"), None),
        P(("dp", "expert"), None),
        P(("dp", "expert"), None),
        P(("dp", "expert"), None),
        P("expert", "dp", None),
        P("expert", "dp", None),
    )
    out_specs = (P("expert", "dp", None), P("expert", "dp", None))

    def fn(*args):
        return body(*args, n_x=n_x, n_y=n_y)

    return jax.shard_map(fn, mesh=mesh, in_specs=in_specs, out_specs=out_specs, check_vma=False)
```
